512 devices in a mesh: tm: 16 (over z, y_hi), space: 32 (over x, y_lo, core).
Axes of the slice: x: 4, y: 8 (y_hi: 2, y_lo: 4; y = y_hi * 4 + y_lo), z: 8, core: 2. Of those that a mesh axis runs over, the one named last changes fastest.
Arguments:
- state: float32 [16, 5, 256, 32, 128], P('tm', None, 'space'), may hold values from -6 to 6
- base: float32 [16, 5, 256, 32, 128], P('tm', None, 'space'), may hold values from -6 to 6
- pseudo_step: float32 [256, 32, 128], P('space'), may hold values from 0.05 to 0.3
- eddy_visc: float32 [256, 32, 128], P('space'), may hold values from 0.02 to 0.2
- jacobians: float32 [3, 5, 5], replicated, may hold values from -2.5 to 2.5
- partner_radial: int32 [2, 256, 128], P(None, 'space'), may hold values from 0 to 127, each once within a row
- partner_instance: int32 [16, 2, 256, 128], P('tm', None, 'space'), may hold values from 0 to 15, as said below
Outputs:
- updated: float32 [16, 5, 256, 32, 128], P('tm', None, 'space')
The draws below stay inside these ranges and needn't reach their ends.
Inputs may be any that keep to these rules, and one draw needn't show every extreme that they name: partner_radial[s, i, :] is a permutation of the radial indices 0..127: the partner cells on the opposite periodic face in the same axial plane. partner_instance[n, 0, i, k] = (n + L_i) mod 16 and partner_instance[n, 1, i, k] = (n - L_i) mod 16 for a lag L_i in 1..15 that depends only on the axial plane i.
All inputs are finite; a program needn't handle non-finite values.
Results may differ from the reference program's by a relative error of at most 0.00005.
Values sent between devices are 32-bit elements; how exact they have to be, the bound alone decides.
No kernel may reach another device: no remote copies, remote signals or barrier semaphores. Data moves between devices by JAX's collectives and lax.ppermute only.
A program may use at most 64 MiB of HBM per device.

```python
import math
import jax
import jax.numpy as jnp
from jax import lax

NV = 5
NT = 16
NJ = 32
NK = 128
NX = 256


def draw_partner_instance(key, part):
    drawn_lags = jax.random.randint(jax.random.fold_in(key, 17), (NX,), 1, NT).astype(jnp.int32)
    plane_ids = jnp.arange(NX, dtype=jnp.int32)
    plane_lags = jnp.where(plane_ids % 3 == 0, NT // 2, drawn_lags).astype(jnp.int32)
    instances = jnp.arange(NT, dtype=jnp.int32)
    lower_side = (instances[:, None] + plane_lags[None, :]) % NT
    upper_side = (instances[:, None] + NT - plane_lags[None, :]) % NT
    paired = jnp.stack([lower_side, upper_side], axis=1).astype(jnp.int32)
    return jnp.broadcast_to(paired[:, :, :, None], (NT, 2, NX, NK)).astype(jnp.int32)


def level_of(stream_key, extent, split, smallest, high):
    level = 1.0
    for axis_at, parts in split:
        draws = jax.random.uniform(jax.random.fold_in(jax.random.fold_in(stream_key, 6), axis_at), (parts,), jnp.float32, smallest / len(split), high / len(split))
        level = level * jnp.repeat(jnp.exp(draws), extent[axis_at] // parts).reshape((-1,) + (1,) * (len(extent) - 1 - axis_at))
    return level


def centred(stream_key, dims, scale, reach, pieces=(), kind=jnp.bfloat16):
    entries = scale * jax.random.normal(stream_key, dims, jnp.float32)
    if pieces:
        entries = entries * level_of(stream_key, dims, pieces, -0.22, 0.18)
    return jnp.clip(entries, -reach, reach).astype(kind)


def setup_inputs(seed: int = 0) -> dict:
    keys = jax.random.split(jax.random.key(seed), 8)
    state = centred(keys[0], (NT, NV, NX, NJ, NK), 1.0, 6.0, ((0, 16), (2, 32)), jnp.float32)
    base = centred(keys[1], (NT, NV, NX, NJ, NK), 1.0, 6.0, ((0, 16), (2, 32)), jnp.float32)
    pseudo_step = jnp.clip(jnp.exp(math.log(0.3) - 1.7917595 * jax.random.uniform(keys[2], (NX, NJ, NK), jnp.float32) ** level_of(keys[2], (NX, NJ, NK), ((0, 32),), -0.2, 0.2)), 0.05, 0.3)
    eddy_visc = jnp.clip(jnp.exp(math.log(0.2) - 2.3025851 * jax.random.uniform(keys[3], (NX, NJ, NK), jnp.float32) ** level_of(keys[3], (NX, NJ, NK), ((0, 32),), -0.2, 0.2)), 0.02, 0.2)
    jacobians = centred(keys[4], (3, NV, NV), NV ** -0.5, 2.5, (), jnp.float32)
    partner_radial = jax.vmap(lambda own: jax.random.permutation(own, NK))(jax.random.split(keys[5], 2 * NX)).reshape((2, NX, NK)).astype(jnp.int32)
    partner_instance = draw_partner_instance(jax.random.fold_in(keys[7], 71), 0)
    return {"state": state, "base": base, "pseudo_step": pseudo_step, "eddy_visc": eddy_visc, "jacobians": jacobians, "partner_radial": partner_radial, "partner_instance": partner_instance}


SECTION_ALPHA = 0.5
PITCH_ANGLE = 2.0 * math.pi / 36.0
NYQUIST_DAMP = 2.0


def time_weights(offset, count):
    offset = offset % count
    angle = math.pi * offset.astype(jnp.float32) / count
    parity = jnp.where((offset % 2) == 1, 1.0, -1.0).astype(jnp.float32)
    sine = jnp.where(offset == 0, 1.0, jnp.sin(angle))
    spectral = 0.5 * parity * jnp.cos(angle) / sine - NYQUIST_DAMP * parity / count
    return jnp.where(offset == 0, NYQUIST_DAMP / count, spectral).astype(jnp.float32)


def rotate_velocity(values, turn):
    cosine = math.cos(PITCH_ANGLE)
    sine = turn * math.sin(PITCH_ANGLE)
    second = values[:, 2]
    third = values[:, 3]
    return jnp.stack([values[:, 0], values[:, 1], cosine * second - sine * third, sine * second + cosine * third, values[:, 4]], axis=1)


def section_update(state, base, pseudo_step, eddy_visc, jacobians, up_i, down_i, low_ghost, high_ghost, time_term):
    up_j = jnp.concatenate([state[:, :, :, 1:], high_ghost[:, :, :, None]], axis=3)
    down_j = jnp.concatenate([low_ghost[:, :, :, None], state[:, :, :, :-1]], axis=3)
    zeros = jnp.zeros(state.shape[:4] + (1,), state.dtype)
    up_k = jnp.concatenate([state[..., 1:], zeros], axis=4)
    down_k = jnp.concatenate([zeros, state[..., :-1]], axis=4)
    diffs = jnp.stack([up_i - down_i, up_j - down_j, up_k - down_k], axis=0) * 0.5
    flux = jnp.einsum("dab,dnbijk->naijk", jacobians, diffs, precision=lax.Precision.HIGHEST)
    laplace = up_i + down_i + up_j + down_j + up_k + down_k - 6.0 * state
    spatial = flux - eddy_visc[None, None] * laplace
    return base - SECTION_ALPHA * pseudo_step[None, None] * (spatial + time_term)


def reference(state, base, pseudo_step, eddy_visc, jacobians, partner_radial, partner_instance):
    count = state.shape[0]
    offsets = jnp.arange(count, dtype=jnp.int32)
    weights = time_weights(offsets[:, None] - offsets[None, :], count)
    time_term = jnp.dot(weights, state.reshape(count, -1), precision=lax.Precision.HIGHEST).reshape(state.shape)
    padded = jnp.pad(state, ((0, 0), (0, 0), (1, 1), (0, 0), (0, 0)))
    up_i = padded[:, :, 2:]
    down_i = padded[:, :, :-2]
    high_face = jnp.transpose(state[:, :, :, -1, :], (0, 2, 3, 1))
    low_face = jnp.transpose(state[:, :, :, 0, :], (0, 2, 3, 1))
    planes = jnp.arange(state.shape[2], dtype=jnp.int32)[None, :, None]
    low_pick = high_face[partner_instance[:, 0], planes, partner_radial[0][None]]
    high_pick = low_face[partner_instance[:, 1], planes, partner_radial[1][None]]
    low_ghost = rotate_velocity(jnp.transpose(low_pick, (0, 3, 1, 2)), -1.0)
    high_ghost = rotate_velocity(jnp.transpose(high_pick, (0, 3, 1, 2)), 1.0)
    return section_update(state, base, pseudo_step, eddy_visc, jacobians, up_i, down_i, low_ghost, high_ghost, time_term)
```

```python
import math

import jax
import jax.numpy as jnp
from jax import lax
from jax.sharding import Mesh
from jax.sharding import PartitionSpec as P

SECTION_ALPHA = 0.5
PITCH_ANGLE = 2.0 * math.pi / 36.0
NYQUIST_DAMP = 2.0
Y_PARTS = 2


def extended_2(block, sides, width):
    for axis, dim in sides:
        count = lax.axis_size(axis)
        forward = [(i, i + 1) for i in range(count - 1)]
        backward = [(target, source) for source, target in forward]
        low = lax.ppermute(
            lax.slice_in_dim(block, block.shape[dim] - width, None, axis=dim), axis, forward
        )
        high = lax.ppermute(lax.slice_in_dim(block, 0, width, axis=dim), axis, backward)
        block = jnp.concatenate([low, block, high], axis=dim)
    return block


def time_weights(offset, count):
    offset = offset % count
    angle = math.pi * offset.astype(jnp.float32) / count
    parity = jnp.where(offset % 2 == 1, 1.0, -1.0).astype(jnp.float32)
    sine = jnp.where(offset == 0, 1.0, jnp.sin(angle))
    spectral = 0.5 * parity * jnp.cos(angle) / sine - NYQUIST_DAMP * parity / count
    return jnp.where(offset == 0, NYQUIST_DAMP / count, spectral)


def rotate_velocity(values, turn):
    cosine = math.cos(PITCH_ANGLE)
    sine = turn * math.sin(PITCH_ANGLE)
    second = values[:, 2]
    third = values[:, 3]
    return jnp.stack(
        [
            values[:, 0],
            values[:, 1],
            cosine * second - sine * third,
            sine * second + cosine * third,
            values[:, 4],
        ],
        axis=1,
    )


def section_update(
    state, base, pseudo_step, eddy_visc, jacobians, up_i, down_i, low_ghost, high_ghost, time_term
):
    up_j = jnp.concatenate([state[:, :, :, 1:], high_ghost[:, :, :, None]], axis=3)
    down_j = jnp.concatenate([low_ghost[:, :, :, None], state[:, :, :, :-1]], axis=3)
    zeros = jnp.zeros(state.shape[:4] + (1,), state.dtype)
    up_k = jnp.concatenate([state[..., 1:], zeros], axis=4)
    down_k = jnp.concatenate([zeros, state[..., :-1]], axis=4)
    diffs = jnp.stack([up_i - down_i, up_j - down_j, up_k - down_k], axis=0) * 0.5
    flux = jnp.einsum("dab,dnbijk->naijk", jacobians, diffs, precision=lax.Precision.HIGHEST)
    laplace = up_i + down_i + up_j + down_j + up_k + down_k - 6.0 * state
    spatial = flux - eddy_visc[None, None] * laplace
    return base - SECTION_ALPHA * pseudo_step[None, None] * (spatial + time_term)


def per_device(state, base, pseudo_step, eddy_visc, jacobians, partner_radial, partner_instance):
    ring = lax.axis_size("tz")
    total_count = ring * Y_PARTS
    z = lax.axis_index("tz")
    y = lax.axis_index("ty")
    own = Y_PARTS * z + y
    partner = own + 1 - 2 * y
    flattened = state.reshape(1, -1)
    gathered = lax.all_gather(flattened, "tz", axis=0, tiled=True)
    held_ids = Y_PARTS * jnp.arange(ring, dtype=jnp.int32) + y
    targets = jnp.stack([own, partner])
    weights = time_weights(targets[:, None] - held_ids[None, :], total_count)
    partial = jnp.dot(weights, gathered, precision=lax.Precision.HIGHEST)

    held = gathered.reshape((ring,) + state.shape[1:])
    faces = jnp.stack([held[:, :, :, -1, :], held[:, :, :, 0, :]], axis=0)
    radial_count = partner_radial.shape[2]
    radial_hot = (partner_radial[..., None] == jnp.arange(radial_count, dtype=jnp.int32)).astype(
        jnp.float32
    )
    remapped = jnp.einsum("szvir,sikr->szvik", faces, radial_hot, precision=lax.Precision.HIGHEST)
    shifts = (targets - own)[:, None, None, None]
    sources = (partner_instance[0][None] + shifts) % total_count
    instance_hot = (sources[..., None] == held_ids).astype(jnp.float32)
    picked = jnp.sum(instance_hot[:, :, None] * jnp.moveaxis(remapped, 1, -1)[None], axis=-1)

    message = jnp.concatenate([partial[1], picked[1].reshape(-1)])
    received = lax.ppermute(message, "ty", [(i, Y_PARTS - 1 - i) for i in range(Y_PARTS)])
    split = partial.shape[1]
    time_term = (partial[0] + received[:split]).reshape(state.shape)
    ghosts = picked[0] + received[split:].reshape(picked.shape[1:])
    low_ghost = rotate_velocity(ghosts[0][None], -1.0)
    high_ghost = rotate_velocity(ghosts[1][None], 1.0)

    extended = extended_2(state, (("space", 2),), 1)
    up_i = extended[:, :, 2:]
    down_i = extended[:, :, :-2]
    return section_update(
        state,
        base,
        pseudo_step,
        eddy_visc,
        jacobians,
        up_i,
        down_i,
        low_ghost,
        high_ghost,
        time_term,
    )


def solution(mesh):
    devices = mesh.devices
    cells = devices.shape[1]
    split_mesh = Mesh(
        devices.reshape(devices.shape[0] // Y_PARTS, Y_PARTS, cells), ("tz", "ty", "space")
    )
    time_axes = ("tz", "ty")
    return jax.shard_map(
        per_device,
        mesh=split_mesh,
        in_specs=(
            P(time_axes, None, "space", None, None),
            P(time_axes, None, "space", None, None),
            P("space", None, None),
            P("space", None, None),
            P(),
            P(None, "space", None),
            P(time_axes, None, "space", None),
        ),
        out_specs=P(time_axes, None, "space", None, None),
        check_vma=False,
    )
```

```python
import math

import jax
import jax.numpy as jnp
from jax import lax
from jax.sharding import Mesh
from jax.sharding import PartitionSpec as P

SECTION_ALPHA = 0.5
PITCH_ANGLE = 2.0 * math.pi / 36.0
NYQUIST_DAMP = 2.0
Y_PARTS = 2


def extended_2(block, sides, width):
    for axis, dim in sides:
        count = lax.axis_size(axis)
        forward = [(i, i + 1) for i in range(count - 1)]
        backward = [(target, source) for source, target in forward]
        low = lax.ppermute(
            lax.slice_in_dim(block, block.shape[dim] - width, None, axis=dim), axis, forward
        )
        high = lax.ppermute(lax.slice_in_dim(block, 0, width, axis=dim), axis, backward)
        block = jnp.concatenate([low, block, high], axis=dim)
    return block


def time_weights(offset, count):
    offset = offset % count
    angle = math.pi * offset.astype(jnp.float32) / count
    parity = jnp.where(offset % 2 == 1, 1.0, -1.0).astype(jnp.float32)
    sine = jnp.where(offset == 0, 1.0, jnp.sin(angle))
    spectral = 0.5 * parity * jnp.cos(angle) / sine - NYQUIST_DAMP * parity / count
    return jnp.where(offset == 0, NYQUIST_DAMP / count, spectral)


def rotate_velocity(values, turn):
    cosine = math.cos(PITCH_ANGLE)
    sine = turn * math.sin(PITCH_ANGLE)
    second = values[:, 2]
    third = values[:, 3]
    return jnp.stack(
        [
            values[:, 0],
            values[:, 1],
            cosine * second - sine * third,
            sine * second + cosine * third,
            values[:, 4],
        ],
        axis=1,
    )


def section_update(
    state, base, pseudo_step, eddy_visc, jacobians, up_i, down_i, low_ghost, high_ghost, time_term
):
    up_j = jnp.concatenate([state[:, :, :, 1:], high_ghost[:, :, :, None]], axis=3)
    down_j = jnp.concatenate([low_ghost[:, :, :, None], state[:, :, :, :-1]], axis=3)
    zeros = jnp.zeros(state.shape[:4] + (1,), state.dtype)
    up_k = jnp.concatenate([state[..., 1:], zeros], axis=4)
    down_k = jnp.concatenate([zeros, state[..., :-1]], axis=4)
    diffs = jnp.stack([up_i - down_i, up_j - down_j, up_k - down_k], axis=0) * 0.5
    flux = jnp.einsum("dab,dnbijk->naijk", jacobians, diffs, precision=lax.Precision.HIGHEST)
    laplace = up_i + down_i + up_j + down_j + up_k + down_k - 6.0 * state
    spatial = flux - eddy_visc[None, None] * laplace
    return base - SECTION_ALPHA * pseudo_step[None, None] * (spatial + time_term)


CHUNKS = 2


def gathered_along_z(block):
    ring = lax.axis_size("tz")
    forward = [(i, (i + 1) % ring) for i in range(ring)]
    backward = [(i, (i - 1) % ring) for i in range(ring)]
    held = [block] + [None] * (ring - 1)
    ahead = block
    behind = block
    for step in range(1, (ring + 1) // 2):
        ahead = lax.ppermute(ahead, "tz", forward)
        behind = lax.ppermute(behind, "tz", backward)
        held[ring - step] = ahead
        held[step] = behind
    if ring % 2 == 0:
        middle = block.shape[3] // 2
        first = lax.ppermute(ahead[:, :, :, :middle], "tz", forward)
        second = lax.ppermute(behind[:, :, :, middle:], "tz", backward)
        held[ring // 2] = jnp.concatenate([first, second], axis=3)
    return jnp.concatenate(held, axis=0)


def chunk_exchange(block, pick_radial, pick_instance, own, partner):
    ring = lax.axis_size("tz")
    total_count = ring * Y_PARTS
    z = lax.axis_index("tz")
    y = lax.axis_index("ty")
    held = gathered_along_z(block)
    held_ids = Y_PARTS * ((z + jnp.arange(ring, dtype=jnp.int32)) % ring) + y
    targets = jnp.stack([own, partner])
    weights = time_weights(targets[:, None] - held_ids[None, :], total_count)
    partial = jnp.sum(weights.reshape((2, ring) + (1,) * (held.ndim - 1)) * held[None], axis=1)

    faces = jnp.stack([held[:, :, :, -1, :], held[:, :, :, 0, :]], axis=0)
    radial_count = pick_radial.shape[2]
    radial_hot = (pick_radial[..., None] == jnp.arange(radial_count, dtype=jnp.int32)).astype(
        jnp.float32
    )
    remapped = jnp.einsum("szvir,sikr->szvik", faces, radial_hot, precision=lax.Precision.HIGHEST)
    shifts = (targets - own)[:, None, None, None]
    sources = (pick_instance[None] + shifts) % total_count
    instance_hot = (sources[..., None] == held_ids).astype(jnp.float32)
    picked = jnp.sum(instance_hot[:, :, None] * jnp.moveaxis(remapped, 1, -1)[None], axis=-1)

    message = jnp.concatenate([partial[1].reshape(-1), picked[1].reshape(-1)])
    return partial, picked, message


def chunk_settle(partial, picked, message):
    received = lax.ppermute(message, "ty", [(i, Y_PARTS - 1 - i) for i in range(Y_PARTS)])
    split = partial[0].size
    time_term = partial[:1] + received[:split].reshape((1,) + partial.shape[1:])
    ghosts = picked[0] + received[split:].reshape(picked.shape[1:])
    return time_term, ghosts


def per_device(state, base, pseudo_step, eddy_visc, jacobians, partner_radial, partner_instance):
    z = lax.axis_index("tz")
    y = lax.axis_index("ty")
    own = Y_PARTS * z + y
    partner = own + 1 - 2 * y
    planes = state.shape[2]
    width = planes // CHUNKS
    time_parts = []
    ghost_parts = []
    message = None
    for chunk in range(CHUNKS):
        window = slice(chunk * width, (chunk + 1) * width)
        block = state[:, :, window]
        if message is not None:
            message, block = lax.optimization_barrier((message, block))
            time_part, ghost_part = chunk_settle(partial, picked, message)
            time_parts.append(time_part)
            ghost_parts.append(ghost_part)
        partial, picked, message = chunk_exchange(
            block,
            partner_radial[:, window],
            partner_instance[0][:, window],
            own,
            partner,
        )
    time_part, ghost_part = chunk_settle(partial, picked, message)
    time_parts.append(time_part)
    ghost_parts.append(ghost_part)
    time_term = jnp.concatenate(time_parts, axis=2)
    ghosts = jnp.concatenate(ghost_parts, axis=2)
    low_ghost = rotate_velocity(ghosts[0][None], -1.0)
    high_ghost = rotate_velocity(ghosts[1][None], 1.0)

    extended = extended_2(state, (("space", 2),), 1)
    up_i = extended[:, :, 2:]
    down_i = extended[:, :, :-2]
    return section_update(
        state,
        base,
        pseudo_step,
        eddy_visc,
        jacobians,
        up_i,
        down_i,
        low_ghost,
        high_ghost,
        time_term,
    )


def solution(mesh):
    devices = mesh.devices
    cells = devices.shape[1]
    split_mesh = Mesh(
        devices.reshape(devices.shape[0] // Y_PARTS, Y_PARTS, cells), ("tz", "ty", "space")
    )
    time_axes = ("tz", "ty")
    return jax.shard_map(
        per_device,
        mesh=split_mesh,
        in_specs=(
            P(time_axes, None, "space", None, None),
            P(time_axes, None, "space", None, None),
            P("space", None, None),
            P("space", None, None),
            P(),
            P(None, "space", None),
            P(time_axes, None, "space", None),
        ),
        out_specs=P(time_axes, None, "space", None, None),
        check_vma=False,
    )
```

```python
import math

import jax
import jax.numpy as jnp
from jax import lax
from jax.sharding import Mesh
from jax.sharding import PartitionSpec as P

SECTION_ALPHA = 0.5
PITCH_ANGLE = 2.0 * math.pi / 36.0
NYQUIST_DAMP = 2.0
Y_PARTS = 2


def extended_2(block, sides, width):
    for axis, dim in sides:
        count = lax.axis_size(axis)
        forward = [(i, i + 1) for i in range(count - 1)]
        backward = [(target, source) for source, target in forward]
        low = lax.ppermute(
            lax.slice_in_dim(block, block.shape[dim] - width, None, axis=dim), axis, forward
        )
        high = lax.ppermute(lax.slice_in_dim(block, 0, width, axis=dim), axis, backward)
        block = jnp.concatenate([low, block, high], axis=dim)
    return block


def time_weights(offset, count):
    offset = offset % count
    angle = math.pi * offset.astype(jnp.float32) / count
    parity = jnp.where(offset % 2 == 1, 1.0, -1.0).astype(jnp.float32)
    sine = jnp.where(offset == 0, 1.0, jnp.sin(angle))
    spectral = 0.5 * parity * jnp.cos(angle) / sine - NYQUIST_DAMP * parity / count
    return jnp.where(offset == 0, NYQUIST_DAMP / count, spectral)


def rotate_velocity(values, turn):
    cosine = math.cos(PITCH_ANGLE)
    sine = turn * math.sin(PITCH_ANGLE)
    second = values[:, 2]
    third = values[:, 3]
    return jnp.stack(
        [
            values[:, 0],
            values[:, 1],
            cosine * second - sine * third,
            sine * second + cosine * third,
            values[:, 4],
        ],
        axis=1,
    )


def section_update(
    state, base, pseudo_step, eddy_visc, jacobians, up_i, down_i, low_ghost, high_ghost, time_term
):
    up_j = jnp.concatenate([state[:, :, :, 1:], high_ghost[:, :, :, None]], axis=3)
    down_j = jnp.concatenate([low_ghost[:, :, :, None], state[:, :, :, :-1]], axis=3)
    zeros = jnp.zeros(state.shape[:4] + (1,), state.dtype)
    up_k = jnp.concatenate([state[..., 1:], zeros], axis=4)
    down_k = jnp.concatenate([zeros, state[..., :-1]], axis=4)
    diffs = jnp.stack([up_i - down_i, up_j - down_j, up_k - down_k], axis=0) * 0.5
    flux = jnp.einsum("dab,dnbijk->naijk", jacobians, diffs, precision=lax.Precision.HIGHEST)
    laplace = up_i + down_i + up_j + down_j + up_k + down_k - 6.0 * state
    spatial = flux - eddy_visc[None, None] * laplace
    return base - SECTION_ALPHA * pseudo_step[None, None] * (spatial + time_term)


def per_device(state, base, pseudo_step, eddy_visc, jacobians, partner_radial, partner_instance):
    ring = lax.axis_size("tz")
    total_count = ring * Y_PARTS
    z = lax.axis_index("tz")
    y = lax.axis_index("ty")
    own = Y_PARTS * z + y
    partner = own + 1 - 2 * y
    swap = [(i, Y_PARTS - 1 - i) for i in range(Y_PARTS)]
    ring_ids = Y_PARTS * jnp.arange(ring, dtype=jnp.int32) + y
    pitch = state.shape[3]
    edge = pitch // 4

    inner = state[:, :, :, edge : pitch - edge]
    other = lax.ppermute(inner, "ty", swap)
    expand = (ring,) + (1,) * (inner.ndim - 1)
    own_weights = time_weights(ring_ids - own, total_count).reshape(expand)
    partner_weights = time_weights(ring_ids - partner, total_count).reshape(expand)
    contributions = own_weights * inner + partner_weights * other
    inner_term = lax.psum_scatter(contributions, "tz", scatter_dimension=0, tiled=True)

    outer = jnp.concatenate([state[:, :, :, :edge], state[:, :, :, pitch - edge :]], axis=3)
    held = lax.all_gather(outer, "tz", axis=0, tiled=True)
    targets = jnp.stack([own, partner])
    weights = time_weights(targets[:, None] - ring_ids[None, :], total_count)
    partial = jnp.sum(weights.reshape((2, ring) + (1,) * (held.ndim - 1)) * held[None], axis=1)

    faces = jnp.stack([held[:, :, :, -1, :], held[:, :, :, 0, :]], axis=0)
    radial_count = partner_radial.shape[2]
    radial_hot = (partner_radial[..., None] == jnp.arange(radial_count, dtype=jnp.int32)).astype(
        jnp.float32
    )
    remapped = jnp.einsum("szvir,sikr->szvik", faces, radial_hot, precision=lax.Precision.HIGHEST)
    shifts = (targets - own)[:, None, None, None]
    sources = (partner_instance[0][None] + shifts) % total_count
    instance_hot = (sources[..., None] == ring_ids).astype(jnp.float32)
    picked = jnp.sum(instance_hot[:, :, None] * jnp.moveaxis(remapped, 1, -1)[None], axis=-1)

    message = jnp.concatenate([partial[1].reshape(-1), picked[1].reshape(-1)])
    received = lax.ppermute(message, "ty", swap)
    split = partial[0].size
    outer_term = partial[:1] + received[:split].reshape((1,) + partial.shape[1:])
    ghosts = picked[0] + received[split:].reshape(picked.shape[1:])
    time_term = jnp.concatenate(
        [outer_term[:, :, :, :edge], inner_term, outer_term[:, :, :, edge:]], axis=3
    )
    low_ghost = rotate_velocity(ghosts[0][None], -1.0)
    high_ghost = rotate_velocity(ghosts[1][None], 1.0)

    extended = extended_2(state, (("space", 2),), 1)
    up_i = extended[:, :, 2:]
    down_i = extended[:, :, :-2]
    return section_update(
        state,
        base,
        pseudo_step,
        eddy_visc,
        jacobians,
        up_i,
        down_i,
        low_ghost,
        high_ghost,
        time_term,
    )


def solution(mesh):
    devices = mesh.devices
    cells = devices.shape[1]
    split_mesh = Mesh(
        devices.reshape(devices.shape[0] // Y_PARTS, Y_PARTS, cells), ("tz", "ty", "space")
    )
    time_axes = ("tz", "ty")
    return jax.shard_map(
        per_device,
        mesh=split_mesh,
        in_specs=(
            P(time_axes, None, "space", None, None),
            P(time_axes, None, "space", None, None),
            P("space", None, None),
            P("space", None, None),
            P(),
            P(None, "space", None),
            P(time_axes, None, "space", None),
        ),
        out_specs=P(time_axes, None, "space", None, None),
        check_vma=False,
    )
```

```python
import math

import jax
import jax.numpy as jnp
from jax import lax
from jax.sharding import Mesh
from jax.sharding import PartitionSpec as P

SECTION_ALPHA = 0.5
PITCH_ANGLE = 2.0 * math.pi / 36.0
NYQUIST_DAMP = 2.0
Y_PARTS = 2


def extended_2(block, sides, width):
    for axis, dim in sides:
        count = lax.axis_size(axis)
        forward = [(i, i + 1) for i in range(count - 1)]
        backward = [(target, source) for source, target in forward]
        low = lax.ppermute(
            lax.slice_in_dim(block, block.shape[dim] - width, None, axis=dim), axis, forward
        )
        high = lax.ppermute(lax.slice_in_dim(block, 0, width, axis=dim), axis, backward)
        block = jnp.concatenate([low, block, high], axis=dim)
    return block


def time_weights(offset, count):
    offset = offset % count
    angle = math.pi * offset.astype(jnp.float32) / count
    parity = jnp.where(offset % 2 == 1, 1.0, -1.0).astype(jnp.float32)
    sine = jnp.where(offset == 0, 1.0, jnp.sin(angle))
    spectral = 0.5 * parity * jnp.cos(angle) / sine - NYQUIST_DAMP * parity / count
    return jnp.where(offset == 0, NYQUIST_DAMP / count, spectral)


def rotate_velocity(values, turn):
    cosine = math.cos(PITCH_ANGLE)
    sine = turn * math.sin(PITCH_ANGLE)
    second = values[:, 2]
    third = values[:, 3]
    return jnp.stack(
        [
            values[:, 0],
            values[:, 1],
            cosine * second - sine * third,
            sine * second + cosine * third,
            values[:, 4],
        ],
        axis=1,
    )


def section_update(
    state, base, pseudo_step, eddy_visc, jacobians, up_i, down_i, low_ghost, high_ghost, time_term
):
    up_j = jnp.concatenate([state[:, :, :, 1:], high_ghost[:, :, :, None]], axis=3)
    down_j = jnp.concatenate([low_ghost[:, :, :, None], state[:, :, :, :-1]], axis=3)
    zeros = jnp.zeros(state.shape[:4] + (1,), state.dtype)
    up_k = jnp.concatenate([state[..., 1:], zeros], axis=4)
    down_k = jnp.concatenate([zeros, state[..., :-1]], axis=4)
    diffs = jnp.stack([up_i - down_i, up_j - down_j, up_k - down_k], axis=0) * 0.5
    flux = jnp.einsum("dab,dnbijk->naijk", jacobians, diffs, precision=lax.Precision.HIGHEST)
    laplace = up_i + down_i + up_j + down_j + up_k + down_k - 6.0 * state
    spatial = flux - eddy_visc[None, None] * laplace
    return base - SECTION_ALPHA * pseudo_step[None, None] * (spatial + time_term)


def reduced_along_z(own_block, partner_block, y, total_count):
    ring = lax.axis_size("tz")
    forward = [(i, (i + 1) % ring) for i in range(ring)]
    backward = [(i, (i - 1) % ring) for i in range(ring)]
    offsets = jnp.arange(ring, dtype=jnp.int32)
    own_weights = time_weights(Y_PARTS * offsets, total_count)
    partner_weights = time_weights(Y_PARTS * offsets + 2 * y - 1, total_count)
    half = own_block.shape[2] // 2
    pieces = (slice(0, half), slice(half, None))

    def contribution(offset, piece):
        k = offset % ring
        return own_weights[k] * own_block[:, :, piece] + partner_weights[k] * partner_block[:, :, piece]

    depth = ring // 2
    depths = {(1, 0): depth, (1, 1): depth - 1, (-1, 0): depth - 1, (-1, 1): depth}
    running = {key: None for key in depths}
    for step in range(1, depth + 1):
        for direction, perm in ((1, forward), (-1, backward)):
            keys = [key for key in depths if key[0] == direction and step <= depths[key]]
            sends = []
            for key in keys:
                term = contribution(direction * (depths[key] - step + 1), pieces[key[1]])
                sends.append(term if running[key] is None else running[key] + term)
            arrived = lax.ppermute(tuple(sends), "tz", perm)
            for key, value in zip(keys, arrived):
                running[key] = value
    halves = [
        running[(1, part)] + running[(-1, part)] for part in range(2)
    ]
    return contribution(0, slice(None)) + jnp.concatenate(halves, axis=2)


def per_device(state, base, pseudo_step, eddy_visc, jacobians, partner_radial, partner_instance):
    ring = lax.axis_size("tz")
    total_count = ring * Y_PARTS
    z = lax.axis_index("tz")
    y = lax.axis_index("ty")
    own = Y_PARTS * z + y
    partner = own + 1 - 2 * y
    swap = [(i, Y_PARTS - 1 - i) for i in range(Y_PARTS)]
    ring_ids = Y_PARTS * jnp.arange(ring, dtype=jnp.int32) + y
    pitch = state.shape[3]
    edge = pitch // 4

    inner = state[:, :, :, edge : pitch - edge]
    other = lax.ppermute(inner, "ty", swap)
    inner_term = reduced_along_z(inner, other, y, total_count)

    outer = jnp.concatenate([state[:, :, :, :edge], state[:, :, :, pitch - edge :]], axis=3)
    held = lax.all_gather(outer, "tz", axis=0, tiled=True)
    targets = jnp.stack([own, partner])
    weights = time_weights(targets[:, None] - ring_ids[None, :], total_count)
    partial = jnp.sum(weights.reshape((2, ring) + (1,) * (held.ndim - 1)) * held[None], axis=1)

    faces = jnp.stack([held[:, :, :, -1, :], held[:, :, :, 0, :]], axis=0)
    radial_count = partner_radial.shape[2]
    radial_hot = (partner_radial[..., None] == jnp.arange(radial_count, dtype=jnp.int32)).astype(
        jnp.float32
    )
    remapped = jnp.einsum("szvir,sikr->szvik", faces, radial_hot, precision=lax.Precision.HIGHEST)
    shifts = (targets - own)[:, None, None, None]
    sources = (partner_instance[0][None] + shifts) % total_count
    instance_hot = (sources[..., None] == ring_ids).astype(jnp.float32)
    picked = jnp.sum(instance_hot[:, :, None] * jnp.moveaxis(remapped, 1, -1)[None], axis=-1)

    message = jnp.concatenate([partial[1].reshape(-1), picked[1].reshape(-1)])
    received = lax.ppermute(message, "ty", swap)
    split = partial[0].size
    outer_term = partial[:1] + received[:split].reshape((1,) + partial.shape[1:])
    ghosts = picked[0] + received[split:].reshape(picked.shape[1:])
    time_term = jnp.concatenate(
        [outer_term[:, :, :, :edge], inner_term, outer_term[:, :, :, edge:]], axis=3
    )
    low_ghost = rotate_velocity(ghosts[0][None], -1.0)
    high_ghost = rotate_velocity(ghosts[1][None], 1.0)

    extended = extended_2(state, (("space", 2),), 1)
    up_i = extended[:, :, 2:]
    down_i = extended[:, :, :-2]
    return section_update(
        state,
        base,
        pseudo_step,
        eddy_visc,
        jacobians,
        up_i,
        down_i,
        low_ghost,
        high_ghost,
        time_term,
    )


def solution(mesh):
    devices = mesh.devices
    cells = devices.shape[1]
    split_mesh = Mesh(
        devices.reshape(devices.shape[0] // Y_PARTS, Y_PARTS, cells), ("tz", "ty", "space")
    )
    time_axes = ("tz", "ty")
    return jax.shard_map(
        per_device,
        mesh=split_mesh,
        in_specs=(
            P(time_axes, None, "space", None, None),
            P(time_axes, None, "space", None, None),
            P("space", None, None),
            P("space", None, None),
            P(),
            P(None, "space", None),
            P(time_axes, None, "space", None),
        ),
        out_specs=P(time_axes, None, "space", None, None),
        check_vma=False,
    )
```

```python
import math

import jax
import jax.numpy as jnp
from jax import lax
from jax.sharding import Mesh
from jax.sharding import PartitionSpec as P

SECTION_ALPHA = 0.5
PITCH_ANGLE = 2.0 * math.pi / 36.0
NYQUIST_DAMP = 2.0
Y_PARTS = 2


def extended_2(block, sides, width):
    for axis, dim in sides:
        count = lax.axis_size(axis)
        forward = [(i, i + 1) for i in range(count - 1)]
        backward = [(target, source) for source, target in forward]
        low = lax.ppermute(
            lax.slice_in_dim(block, block.shape[dim] - width, None, axis=dim), axis, forward
        )
        high = lax.ppermute(lax.slice_in_dim(block, 0, width, axis=dim), axis, backward)
        block = jnp.concatenate([low, block, high], axis=dim)
    return block


def time_weights(offset, count):
    offset = offset % count
    angle = math.pi * offset.astype(jnp.float32) / count
    parity = jnp.where(offset % 2 == 1, 1.0, -1.0).astype(jnp.float32)
    sine = jnp.where(offset == 0, 1.0, jnp.sin(angle))
    spectral = 0.5 * parity * jnp.cos(angle) / sine - NYQUIST_DAMP * parity / count
    return jnp.where(offset == 0, NYQUIST_DAMP / count, spectral)


def rotate_velocity(values, turn):
    cosine = math.cos(PITCH_ANGLE)
    sine = turn * math.sin(PITCH_ANGLE)
    second = values[:, 2]
    third = values[:, 3]
    return jnp.stack(
        [
            values[:, 0],
            values[:, 1],
            cosine * second - sine * third,
            sine * second + cosine * third,
            values[:, 4],
        ],
        axis=1,
    )


def section_spatial(state, eddy_visc, jacobians, up_i, down_i, low_ghost, high_ghost):
    up_j = jnp.concatenate([state[:, :, :, 1:], high_ghost[:, :, :, None]], axis=3)
    down_j = jnp.concatenate([low_ghost[:, :, :, None], state[:, :, :, :-1]], axis=3)
    zeros = jnp.zeros(state.shape[:4] + (1,), state.dtype)
    up_k = jnp.concatenate([state[..., 1:], zeros], axis=4)
    down_k = jnp.concatenate([zeros, state[..., :-1]], axis=4)
    diffs = [(up_i - down_i) * 0.5, (up_j - down_j) * 0.5, (up_k - down_k) * 0.5]
    rows = []
    for target in range(state.shape[1]):
        total = None
        for direction, diff in enumerate(diffs):
            for source in range(state.shape[1]):
                term = jacobians[direction, target, source] * diff[:, source]
                total = term if total is None else total + term
        rows.append(total)
    flux = jnp.stack(rows, axis=1)
    laplace = up_i + down_i + up_j + down_j + up_k + down_k - 6.0 * state
    return flux - eddy_visc[None, None] * laplace


def per_device(state, base, pseudo_step, eddy_visc, jacobians, partner_radial, partner_instance):
    ring = lax.axis_size("tz")
    total_count = ring * Y_PARTS
    z = lax.axis_index("tz")
    y = lax.axis_index("ty")
    own = Y_PARTS * z + y
    partner = own + 1 - 2 * y
    swap = [(i, Y_PARTS - 1 - i) for i in range(Y_PARTS)]
    ring_ids = Y_PARTS * jnp.arange(ring, dtype=jnp.int32) + y
    pitch = state.shape[3]
    edge = pitch // 4

    inner = state[:, :, :, edge : pitch - edge]
    other = lax.ppermute(inner, "ty", swap)
    expand = (ring,) + (1,) * (inner.ndim - 1)
    own_weights = time_weights(ring_ids - own, total_count).reshape(expand)
    partner_weights = time_weights(ring_ids - partner, total_count).reshape(expand)
    contributions = own_weights * inner + partner_weights * other
    inner_term = lax.psum_scatter(contributions, "tz", scatter_dimension=0, tiled=True)

    outer = jnp.concatenate([state[:, :, :, :edge], state[:, :, :, pitch - edge :]], axis=3)
    held = lax.all_gather(outer, "tz", axis=0, tiled=True)
    targets = jnp.stack([own, partner])
    weights = time_weights(targets[:, None] - ring_ids[None, :], total_count)
    partial = jnp.sum(weights.reshape((2, ring) + (1,) * (held.ndim - 1)) * held[None], axis=1)

    faces = jnp.stack([held[:, :, :, -1, :], held[:, :, :, 0, :]], axis=0)
    radial_count = partner_radial.shape[2]
    radial_hot = (partner_radial[..., None] == jnp.arange(radial_count, dtype=jnp.int32)).astype(
        jnp.float32
    )
    remapped = jnp.einsum("szvir,sikr->szvik", faces, radial_hot, precision=lax.Precision.HIGHEST)
    shifts = (targets - own)[:, None, None, None]
    sources = (partner_instance[0][None] + shifts) % total_count
    instance_hot = (sources[..., None] == ring_ids).astype(jnp.float32)
    picked = jnp.sum(instance_hot[:, :, None] * jnp.moveaxis(remapped, 1, -1)[None], axis=-1)

    message = jnp.concatenate([partial[1].reshape(-1), picked[1].reshape(-1)])
    received = lax.ppermute(message, "ty", swap)
    split = partial[0].size
    outer_term = partial[:1] + received[:split].reshape((1,) + partial.shape[1:])
    ghosts = picked[0] + received[split:].reshape(picked.shape[1:])
    time_term = jnp.concatenate(
        [outer_term[:, :, :, :edge], inner_term, outer_term[:, :, :, edge:]], axis=3
    )
    low_ghost = rotate_velocity(ghosts[0][None], -1.0)
    high_ghost = rotate_velocity(ghosts[1][None], 1.0)

    extended = extended_2(state, (("space", 2),), 1)
    up_i = extended[:, :, 2:]
    down_i = extended[:, :, :-2]
    spatial = lax.optimization_barrier(
        section_spatial(state, eddy_visc, jacobians, up_i, down_i, low_ghost, high_ghost)
    )
    return base - SECTION_ALPHA * pseudo_step[None, None] * (spatial + time_term)


def solution(mesh):
    devices = mesh.devices
    cells = devices.shape[1]
    split_mesh = Mesh(
        devices.reshape(devices.shape[0] // Y_PARTS, Y_PARTS, cells), ("tz", "ty", "space")
    )
    time_axes = ("tz", "ty")
    return jax.shard_map(
        per_device,
        mesh=split_mesh,
        in_specs=(
            P(time_axes, None, "space", None, None),
            P(time_axes, None, "space", None, None),
            P("space", None, None),
            P("space", None, None),
            P(),
            P(None, "space", None),
            P(time_axes, None, "space", None),
        ),
        out_specs=P(time_axes, None, "space", None, None),
        check_vma=False,
    )
```

```python
import math

import jax
import jax.numpy as jnp
from jax import lax
from jax.sharding import Mesh
from jax.sharding import PartitionSpec as P

SECTION_ALPHA = 0.5
PITCH_ANGLE = 2.0 * math.pi / 36.0
NYQUIST_DAMP = 2.0
Y_PARTS = 2


def extended_2(block, sides, width):
    for axis, dim in sides:
        count = lax.axis_size(axis)
        forward = [(i, i + 1) for i in range(count - 1)]
        backward = [(target, source) for source, target in forward]
        low = lax.ppermute(
            lax.slice_in_dim(block, block.shape[dim] - width, None, axis=dim), axis, forward
        )
        high = lax.ppermute(lax.slice_in_dim(block, 0, width, axis=dim), axis, backward)
        block = jnp.concatenate([low, block, high], axis=dim)
    return block


def time_weights(offset, count):
    offset = offset % count
    angle = math.pi * offset.astype(jnp.float32) / count
    parity = jnp.where(offset % 2 == 1, 1.0, -1.0).astype(jnp.float32)
    sine = jnp.where(offset == 0, 1.0, jnp.sin(angle))
    spectral = 0.5 * parity * jnp.cos(angle) / sine - NYQUIST_DAMP * parity / count
    return jnp.where(offset == 0, NYQUIST_DAMP / count, spectral)


def rotate_velocity(values, turn):
    cosine = math.cos(PITCH_ANGLE)
    sine = turn * math.sin(PITCH_ANGLE)
    second = values[:, 2]
    third = values[:, 3]
    return jnp.stack(
        [
            values[:, 0],
            values[:, 1],
            cosine * second - sine * third,
            sine * second + cosine * third,
            values[:, 4],
        ],
        axis=1,
    )


def section_spatial(state, eddy_visc, jacobians, up_i, down_i, low_ghost, high_ghost):
    up_j = jnp.concatenate([state[:, :, :, 1:], high_ghost[:, :, :, None]], axis=3)
    down_j = jnp.concatenate([low_ghost[:, :, :, None], state[:, :, :, :-1]], axis=3)
    zeros = jnp.zeros(state.shape[:4] + (1,), state.dtype)
    up_k = jnp.concatenate([state[..., 1:], zeros], axis=4)
    down_k = jnp.concatenate([zeros, state[..., :-1]], axis=4)
    diffs = [(up_i - down_i) * 0.5, (up_j - down_j) * 0.5, (up_k - down_k) * 0.5]
    flux = None
    for direction, diff in enumerate(diffs):
        for source in range(state.shape[1]):
            column = jacobians[direction, :, source].reshape((1, -1) + (1,) * (state.ndim - 2))
            term = column * diff[:, source : source + 1]
            flux = term if flux is None else flux + term
    laplace = up_i + down_i + up_j + down_j + up_k + down_k - 6.0 * state
    return flux - eddy_visc[None, None] * laplace


def per_device(state, base, pseudo_step, eddy_visc, jacobians, partner_radial, partner_instance):
    ring = lax.axis_size("tz")
    total_count = ring * Y_PARTS
    z = lax.axis_index("tz")
    y = lax.axis_index("ty")
    own = Y_PARTS * z + y
    partner = own + 1 - 2 * y
    swap = [(i, Y_PARTS - 1 - i) for i in range(Y_PARTS)]
    ring_ids = Y_PARTS * jnp.arange(ring, dtype=jnp.int32) + y
    pitch = state.shape[3]
    edge = pitch // 4

    inner = state[:, :, :, edge : pitch - edge]
    other = lax.ppermute(inner, "ty", swap)
    expand = (ring,) + (1,) * (inner.ndim - 1)
    own_weights = time_weights(ring_ids - own, total_count).reshape(expand)
    partner_weights = time_weights(ring_ids - partner, total_count).reshape(expand)
    contributions = own_weights * inner + partner_weights * other
    inner_term = lax.psum_scatter(contributions, "tz", scatter_dimension=0, tiled=True)

    outer = jnp.concatenate([state[:, :, :, :edge], state[:, :, :, pitch - edge :]], axis=3)
    held = lax.all_gather(outer, "tz", axis=0, tiled=True)
    targets = jnp.stack([own, partner])
    weights = time_weights(targets[:, None] - ring_ids[None, :], total_count)
    partial = jnp.sum(weights.reshape((2, ring) + (1,) * (held.ndim - 1)) * held[None], axis=1)

    faces = jnp.stack([held[:, :, :, -1, :], held[:, :, :, 0, :]], axis=0)
    radial_count = partner_radial.shape[2]
    radial_hot = (partner_radial[..., None] == jnp.arange(radial_count, dtype=jnp.int32)).astype(
        jnp.float32
    )
    remapped = jnp.einsum("szvir,sikr->szvik", faces, radial_hot, precision=lax.Precision.HIGHEST)
    shifts = (targets - own)[:, None, None, None]
    sources = (partner_instance[0][None] + shifts) % total_count
    instance_hot = (sources[..., None] == ring_ids).astype(jnp.float32)
    picked = jnp.sum(instance_hot[:, :, None] * jnp.moveaxis(remapped, 1, -1)[None], axis=-1)

    message = jnp.concatenate([partial[1].reshape(-1), picked[1].reshape(-1)])
    received = lax.ppermute(message, "ty", swap)
    split = partial[0].size
    outer_term = partial[:1] + received[:split].reshape((1,) + partial.shape[1:])
    ghosts = picked[0] + received[split:].reshape(picked.shape[1:])
    time_term = jnp.concatenate(
        [outer_term[:, :, :, :edge], inner_term, outer_term[:, :, :, edge:]], axis=3
    )
    low_ghost = rotate_velocity(ghosts[0][None], -1.0)
    high_ghost = rotate_velocity(ghosts[1][None], 1.0)

    extended = extended_2(state, (("space", 2),), 1)
    up_i = extended[:, :, 2:]
    down_i = extended[:, :, :-2]
    spatial = lax.optimization_barrier(
        section_spatial(state, eddy_visc, jacobians, up_i, down_i, low_ghost, high_ghost)
    )
    return base - SECTION_ALPHA * pseudo_step[None, None] * (spatial + time_term)


def solution(mesh):
    devices = mesh.devices
    cells = devices.shape[1]
    split_mesh = Mesh(
        devices.reshape(devices.shape[0] // Y_PARTS, Y_PARTS, cells), ("tz", "ty", "space")
    )
    time_axes = ("tz", "ty")
    return jax.shard_map(
        per_device,
        mesh=split_mesh,
        in_specs=(
            P(time_axes, None, "space", None, None),
            P(time_axes, None, "space", None, None),
            P("space", None, None),
            P("space", None, None),
            P(),
            P(None, "space", None),
            P(time_axes, None, "space", None),
        ),
        out_specs=P(time_axes, None, "space", None, None),
        check_vma=False,
    )
```

```python
import math

import jax
import jax.numpy as jnp
from jax import lax
from jax.sharding import Mesh
from jax.sharding import PartitionSpec as P

SECTION_ALPHA = 0.5
PITCH_ANGLE = 2.0 * math.pi / 36.0
NYQUIST_DAMP = 2.0
Y_PARTS = 2


def extended_2(block, sides, width):
    for axis, dim in sides:
        count = lax.axis_size(axis)
        forward = [(i, i + 1) for i in range(count - 1)]
        backward = [(target, source) for source, target in forward]
        low = lax.ppermute(
            lax.slice_in_dim(block, block.shape[dim] - width, None, axis=dim), axis, forward
        )
        high = lax.ppermute(lax.slice_in_dim(block, 0, width, axis=dim), axis, backward)
        block = jnp.concatenate([low, block, high], axis=dim)
    return block


def time_weights(offset, count):
    offset = offset % count
    angle = math.pi * offset.astype(jnp.float32) / count
    parity = jnp.where(offset % 2 == 1, 1.0, -1.0).astype(jnp.float32)
    sine = jnp.where(offset == 0, 1.0, jnp.sin(angle))
    spectral = 0.5 * parity * jnp.cos(angle) / sine - NYQUIST_DAMP * parity / count
    return jnp.where(offset == 0, NYQUIST_DAMP / count, spectral)


def rotate_velocity(values, turn):
    cosine = math.cos(PITCH_ANGLE)
    sine = turn * math.sin(PITCH_ANGLE)
    second = values[:, 2]
    third = values[:, 3]
    return jnp.stack(
        [
            values[:, 0],
            values[:, 1],
            cosine * second - sine * third,
            sine * second + cosine * third,
            values[:, 4],
        ],
        axis=1,
    )


def section_spatial(state, eddy_visc, jacobians, up_i, down_i, low_ghost, high_ghost):
    up_j = jnp.concatenate([state[:, :, :, 1:], high_ghost[:, :, :, None]], axis=3)
    down_j = jnp.concatenate([low_ghost[:, :, :, None], state[:, :, :, :-1]], axis=3)
    zeros = jnp.zeros(state.shape[:4] + (1,), state.dtype)
    up_k = jnp.concatenate([state[..., 1:], zeros], axis=4)
    down_k = jnp.concatenate([zeros, state[..., :-1]], axis=4)
    diffs = [(up_i - down_i) * 0.5, (up_j - down_j) * 0.5, (up_k - down_k) * 0.5]
    flux = None
    for direction, diff in enumerate(diffs):
        for source in range(state.shape[1]):
            column = jacobians[direction, :, source].reshape((1, -1) + (1,) * (state.ndim - 2))
            term = column * diff[:, source : source + 1]
            flux = term if flux is None else flux + term
    laplace = up_i + down_i + up_j + down_j + up_k + down_k - 6.0 * state
    return flux - eddy_visc[None, None] * laplace


def reduced_along_z(own_block, partner_block, y, total_count):
    ring = lax.axis_size("tz")
    forward = [(i, (i + 1) % ring) for i in range(ring)]
    backward = [(i, (i - 1) % ring) for i in range(ring)]
    offsets = jnp.arange(ring, dtype=jnp.int32)
    expand = (ring,) + (1,) * own_block.ndim
    own_weights = time_weights(Y_PARTS * offsets, total_count).reshape(expand)
    partner_weights = time_weights(Y_PARTS * offsets + 2 * y - 1, total_count).reshape(expand)
    terms = own_weights * own_block[None] + partner_weights * partner_block[None]
    half = own_block.shape[2] // 2
    depth = ring // 2

    def addend(first, second):
        return jnp.concatenate([terms[first][:, :, :half], terms[second][:, :, half:]], axis=2)

    ahead = None
    behind = None
    for step in range(1, depth):
        sent = addend(depth - step + 1, depth - step)
        ahead = lax.ppermute(sent if ahead is None else ahead + sent, "tz", forward)
        sent = addend(ring - depth + step, ring - depth - 1 + step)
        behind = lax.ppermute(sent if behind is None else behind + sent, "tz", backward)
    far_ahead = lax.ppermute(ahead[:, :, :half] + terms[1][:, :, :half], "tz", forward)
    far_behind = lax.ppermute(behind[:, :, half:] + terms[ring - 1][:, :, half:], "tz", backward)
    first = far_ahead + behind[:, :, :half]
    second = ahead[:, :, half:] + far_behind
    return terms[0] + jnp.concatenate([first, second], axis=2)


def per_device(state, base, pseudo_step, eddy_visc, jacobians, partner_radial, partner_instance):
    ring = lax.axis_size("tz")
    total_count = ring * Y_PARTS
    z = lax.axis_index("tz")
    y = lax.axis_index("ty")
    own = Y_PARTS * z + y
    partner = own + 1 - 2 * y
    swap = [(i, Y_PARTS - 1 - i) for i in range(Y_PARTS)]
    ring_ids = Y_PARTS * jnp.arange(ring, dtype=jnp.int32) + y
    pitch = state.shape[3]
    edge = pitch // 4

    inner = state[:, :, :, edge : pitch - edge]
    other = lax.ppermute(inner, "ty", swap)
    inner_term = reduced_along_z(inner, other, y, total_count)

    outer = jnp.concatenate([state[:, :, :, :edge], state[:, :, :, pitch - edge :]], axis=3)
    held = lax.all_gather(outer, "tz", axis=0, tiled=True)
    targets = jnp.stack([own, partner])
    weights = time_weights(targets[:, None] - ring_ids[None, :], total_count)
    partial = jnp.sum(weights.reshape((2, ring) + (1,) * (held.ndim - 1)) * held[None], axis=1)

    faces = jnp.stack([held[:, :, :, -1, :], held[:, :, :, 0, :]], axis=0)
    radial_count = partner_radial.shape[2]
    radial_hot = (partner_radial[..., None] == jnp.arange(radial_count, dtype=jnp.int32)).astype(
        jnp.float32
    )
    remapped = jnp.einsum("szvir,sikr->szvik", faces, radial_hot, precision=lax.Precision.HIGHEST)
    shifts = (targets - own)[:, None, None, None]
    sources = (partner_instance[0][None] + shifts) % total_count
    instance_hot = (sources[..., None] == ring_ids).astype(jnp.float32)
    picked = jnp.sum(instance_hot[:, :, None] * jnp.moveaxis(remapped, 1, -1)[None], axis=-1)

    message = jnp.concatenate([partial[1].reshape(-1), picked[1].reshape(-1)])
    received = lax.ppermute(message, "ty", swap)
    split = partial[0].size
    outer_term = partial[:1] + received[:split].reshape((1,) + partial.shape[1:])
    ghosts = picked[0] + received[split:].reshape(picked.shape[1:])
    time_term = jnp.concatenate(
        [outer_term[:, :, :, :edge], inner_term, outer_term[:, :, :, edge:]], axis=3
    )
    low_ghost = rotate_velocity(ghosts[0][None], -1.0)
    high_ghost = rotate_velocity(ghosts[1][None], 1.0)

    extended = extended_2(state, (("space", 2),), 1)
    up_i = extended[:, :, 2:]
    down_i = extended[:, :, :-2]
    spatial = lax.optimization_barrier(
        section_spatial(state, eddy_visc, jacobians, up_i, down_i, low_ghost, high_ghost)
    )
    return base - SECTION_ALPHA * pseudo_step[None, None] * (spatial + time_term)


def solution(mesh):
    devices = mesh.devices
    cells = devices.shape[1]
    split_mesh = Mesh(
        devices.reshape(devices.shape[0] // Y_PARTS, Y_PARTS, cells), ("tz", "ty", "space")
    )
    time_axes = ("tz", "ty")
    return jax.shard_map(
        per_device,
        mesh=split_mesh,
        in_specs=(
            P(time_axes, None, "space", None, None),
            P(time_axes, None, "space", None, None),
            P("space", None, None),
            P("space", None, None),
            P(),
            P(None, "space", None),
            P(time_axes, None, "space", None),
        ),
        out_specs=P(time_axes, None, "space", None, None),
        check_vma=False,
    )
```

```python
import math

import jax
import jax.numpy as jnp
from jax import lax
from jax.sharding import Mesh
from jax.sharding import PartitionSpec as P

SECTION_ALPHA = 0.5
PITCH_ANGLE = 2.0 * math.pi / 36.0
NYQUIST_DAMP = 2.0
Y_PARTS = 2


def extended_2(block, sides, width):
    for axis, dim in sides:
        count = lax.axis_size(axis)
        forward = [(i, i + 1) for i in range(count - 1)]
        backward = [(target, source) for source, target in forward]
        low = lax.ppermute(
            lax.slice_in_dim(block, block.shape[dim] - width, None, axis=dim), axis, forward
        )
        high = lax.ppermute(lax.slice_in_dim(block, 0, width, axis=dim), axis, backward)
        block = jnp.concatenate([low, block, high], axis=dim)
    return block


def time_weights(offset, count):
    offset = offset % count
    angle = math.pi * offset.astype(jnp.float32) / count
    parity = jnp.where(offset % 2 == 1, 1.0, -1.0).astype(jnp.float32)
    sine = jnp.where(offset == 0, 1.0, jnp.sin(angle))
    spectral = 0.5 * parity * jnp.cos(angle) / sine - NYQUIST_DAMP * parity / count
    return jnp.where(offset == 0, NYQUIST_DAMP / count, spectral)


def rotate_velocity(values, turn):
    cosine = math.cos(PITCH_ANGLE)
    sine = turn * math.sin(PITCH_ANGLE)
    second = values[:, 2]
    third = values[:, 3]
    return jnp.stack(
        [
            values[:, 0],
            values[:, 1],
            cosine * second - sine * third,
            sine * second + cosine * third,
            values[:, 4],
        ],
        axis=1,
    )


def section_spatial(state, eddy_visc, jacobians, up_i, down_i, low_ghost, high_ghost):
    up_j = jnp.concatenate([state[:, :, :, 1:], high_ghost[:, :, :, None]], axis=3)
    down_j = jnp.concatenate([low_ghost[:, :, :, None], state[:, :, :, :-1]], axis=3)
    zeros = jnp.zeros(state.shape[:4] + (1,), state.dtype)
    up_k = jnp.concatenate([state[..., 1:], zeros], axis=4)
    down_k = jnp.concatenate([zeros, state[..., :-1]], axis=4)
    diffs = [(up_i - down_i) * 0.5, (up_j - down_j) * 0.5, (up_k - down_k) * 0.5]
    flux = None
    for direction, diff in enumerate(diffs):
        for source in range(state.shape[1]):
            column = jacobians[direction, :, source].reshape((1, -1) + (1,) * (state.ndim - 2))
            term = column * diff[:, source : source + 1]
            flux = term if flux is None else flux + term
    laplace = up_i + down_i + up_j + down_j + up_k + down_k - 6.0 * state
    return flux - eddy_visc[None, None] * laplace


def reduced_along_z(own_block, partner_block, y, total_count):
    ring = lax.axis_size("tz")
    forward = [(i, (i + 1) % ring) for i in range(ring)]
    backward = [(i, (i - 1) % ring) for i in range(ring)]
    offsets = jnp.arange(ring, dtype=jnp.int32)
    expand = (ring,) + (1,) * own_block.ndim
    own_weights = time_weights(Y_PARTS * offsets, total_count).reshape(expand)
    partner_weights = time_weights(Y_PARTS * offsets + 2 * y - 1, total_count).reshape(expand)
    terms = own_weights * own_block[None] + partner_weights * partner_block[None]
    half = own_block.shape[2] // 2
    depth = ring // 2

    def addend(first, second):
        return jnp.concatenate([terms[first][:, :, :half], terms[second][:, :, half:]], axis=2)

    ahead = None
    behind = None
    for step in range(1, depth):
        sent = addend(depth - step + 1, depth - step)
        ahead = lax.ppermute(sent if ahead is None else ahead + sent, "tz", forward)
        sent = addend(ring - depth + step, ring - depth - 1 + step)
        behind = lax.ppermute(sent if behind is None else behind + sent, "tz", backward)
    far_ahead = lax.ppermute(ahead[:, :, :half] + terms[1][:, :, :half], "tz", forward)
    far_behind = lax.ppermute(behind[:, :, half:] + terms[ring - 1][:, :, half:], "tz", backward)
    first = far_ahead + behind[:, :, :half]
    second = ahead[:, :, half:] + far_behind
    return terms[0] + jnp.concatenate([first, second], axis=2)


def per_device(state, base, pseudo_step, eddy_visc, jacobians, partner_radial, partner_instance):
    ring = lax.axis_size("tz")
    total_count = ring * Y_PARTS
    z = lax.axis_index("tz")
    y = lax.axis_index("ty")
    own = Y_PARTS * z + y
    partner = own + 1 - 2 * y
    swap = [(i, Y_PARTS - 1 - i) for i in range(Y_PARTS)]
    ring_ids = Y_PARTS * jnp.arange(ring, dtype=jnp.int32) + y
    pitch = state.shape[3]
    edge = pitch // 4

    inner = state[:, :, :, edge : pitch - edge]
    other = lax.ppermute(inner, "ty", swap)
    expand = (ring,) + (1,) * (inner.ndim - 1)
    own_weights = time_weights(ring_ids - own, total_count).reshape(expand)
    partner_weights = time_weights(ring_ids - partner, total_count).reshape(expand)
    contributions = own_weights * inner[:, :, :, :edge] + partner_weights * other[:, :, :, :edge]
    scattered_term = lax.psum_scatter(contributions, "tz", scatter_dimension=0, tiled=True)
    ring_term = reduced_along_z(inner[:, :, :, edge:], other[:, :, :, edge:], y, total_count)
    inner_term = jnp.concatenate([scattered_term, ring_term], axis=3)

    outer = jnp.concatenate([state[:, :, :, :edge], state[:, :, :, pitch - edge :]], axis=3)
    held = lax.all_gather(outer, "tz", axis=0, tiled=True)
    targets = jnp.stack([own, partner])
    weights = time_weights(targets[:, None] - ring_ids[None, :], total_count)
    partial = jnp.sum(weights.reshape((2, ring) + (1,) * (held.ndim - 1)) * held[None], axis=1)

    faces = jnp.stack([held[:, :, :, -1, :], held[:, :, :, 0, :]], axis=0)
    radial_count = partner_radial.shape[2]
    radial_hot = (partner_radial[..., None] == jnp.arange(radial_count, dtype=jnp.int32)).astype(
        jnp.float32
    )
    remapped = jnp.einsum("szvir,sikr->szvik", faces, radial_hot, precision=lax.Precision.HIGHEST)
    shifts = (targets - own)[:, None, None, None]
    sources = (partner_instance[0][None] + shifts) % total_count
    instance_hot = (sources[..., None] == ring_ids).astype(jnp.float32)
    picked = jnp.sum(instance_hot[:, :, None] * jnp.moveaxis(remapped, 1, -1)[None], axis=-1)

    message = jnp.concatenate([partial[1].reshape(-1), picked[1].reshape(-1)])
    received = lax.ppermute(message, "ty", swap)
    split = partial[0].size
    outer_term = partial[:1] + received[:split].reshape((1,) + partial.shape[1:])
    ghosts = picked[0] + received[split:].reshape(picked.shape[1:])
    time_term = jnp.concatenate(
        [outer_term[:, :, :, :edge], inner_term, outer_term[:, :, :, edge:]], axis=3
    )
    low_ghost = rotate_velocity(ghosts[0][None], -1.0)
    high_ghost = rotate_velocity(ghosts[1][None], 1.0)

    extended = extended_2(state, (("space", 2),), 1)
    up_i = extended[:, :, 2:]
    down_i = extended[:, :, :-2]
    spatial = lax.optimization_barrier(
        section_spatial(state, eddy_visc, jacobians, up_i, down_i, low_ghost, high_ghost)
    )
    return base - SECTION_ALPHA * pseudo_step[None, None] * (spatial + time_term)


def solution(mesh):
    devices = mesh.devices
    cells = devices.shape[1]
    split_mesh = Mesh(
        devices.reshape(devices.shape[0] // Y_PARTS, Y_PARTS, cells), ("tz", "ty", "space")
    )
    time_axes = ("tz", "ty")
    return jax.shard_map(
        per_device,
        mesh=split_mesh,
        in_specs=(
            P(time_axes, None, "space", None, None),
            P(time_axes, None, "space", None, None),
            P("space", None, None),
            P("space", None, None),
            P(),
            P(None, "space", None),
            P(time_axes, None, "space", None),
        ),
        out_specs=P(time_axes, None, "space", None, None),
        check_vma=False,
    )
```

```python
import math

import jax
import jax.numpy as jnp
from jax import lax
from jax.sharding import Mesh
from jax.sharding import PartitionSpec as P

SECTION_ALPHA = 0.5
PITCH_ANGLE = 2.0 * math.pi / 36.0
NYQUIST_DAMP = 2.0
Y_PARTS = 2


def extended_2(block, sides, width):
    for axis, dim in sides:
        count = lax.axis_size(axis)
        forward = [(i, i + 1) for i in range(count - 1)]
        backward = [(target, source) for source, target in forward]
        low = lax.ppermute(
            lax.slice_in_dim(block, block.shape[dim] - width, None, axis=dim), axis, forward
        )
        high = lax.ppermute(lax.slice_in_dim(block, 0, width, axis=dim), axis, backward)
        block = jnp.concatenate([low, block, high], axis=dim)
    return block


def time_weights(offset, count):
    offset = offset % count
    angle = math.pi * offset.astype(jnp.float32) / count
    parity = jnp.where(offset % 2 == 1, 1.0, -1.0).astype(jnp.float32)
    sine = jnp.where(offset == 0, 1.0, jnp.sin(angle))
    spectral = 0.5 * parity * jnp.cos(angle) / sine - NYQUIST_DAMP * parity / count
    return jnp.where(offset == 0, NYQUIST_DAMP / count, spectral)


def rotate_velocity(values, turn):
    cosine = math.cos(PITCH_ANGLE)
    sine = turn * math.sin(PITCH_ANGLE)
    second = values[:, 2]
    third = values[:, 3]
    return jnp.stack(
        [
            values[:, 0],
            values[:, 1],
            cosine * second - sine * third,
            sine * second + cosine * third,
            values[:, 4],
        ],
        axis=1,
    )


def section_spatial(state, eddy_visc, jacobians, up_i, down_i, low_ghost, high_ghost):
    up_j = jnp.concatenate([state[:, :, :, 1:], high_ghost[:, :, :, None]], axis=3)
    down_j = jnp.concatenate([low_ghost[:, :, :, None], state[:, :, :, :-1]], axis=3)
    zeros = jnp.zeros(state.shape[:4] + (1,), state.dtype)
    up_k = jnp.concatenate([state[..., 1:], zeros], axis=4)
    down_k = jnp.concatenate([zeros, state[..., :-1]], axis=4)
    diffs = [(up_i - down_i) * 0.5, (up_j - down_j) * 0.5, (up_k - down_k) * 0.5]
    flux = None
    for direction, diff in enumerate(diffs):
        for source in range(state.shape[1]):
            column = jacobians[direction, :, source].reshape((1, -1) + (1,) * (state.ndim - 2))
            term = column * diff[:, source : source + 1]
            flux = term if flux is None else flux + term
    laplace = up_i + down_i + up_j + down_j + up_k + down_k - 6.0 * state
    return flux - eddy_visc[None, None] * laplace


def per_device(state, base, pseudo_step, eddy_visc, jacobians, partner_radial, partner_instance):
    ring = lax.axis_size("tz")
    total_count = ring * Y_PARTS
    z = lax.axis_index("tz")
    y = lax.axis_index("ty")
    own = Y_PARTS * z + y
    partner = own + 1 - 2 * y
    swap = [(i, Y_PARTS - 1 - i) for i in range(Y_PARTS)]
    ring_ids = Y_PARTS * jnp.arange(ring, dtype=jnp.int32) + y
    pitch = state.shape[3]
    edge = pitch // 4

    inner = state[:, :, :, edge : pitch - edge]
    other = lax.ppermute(inner, "ty", swap)
    expand = (ring,) + (1,) * (inner.ndim - 1)
    own_weights = time_weights(ring_ids - own, total_count).reshape(expand)
    partner_weights = time_weights(ring_ids - partner, total_count).reshape(expand)
    contributions = own_weights * inner + partner_weights * other
    inner_term = lax.psum_scatter(contributions, "tz", scatter_dimension=0, tiled=True)

    groups = pitch // edge
    grouped = state.reshape(state.shape[:3] + (groups, edge, state.shape[4]))
    outer = grouped[:, :, :, :: groups - 1].reshape(state.shape[:3] + (2 * edge, state.shape[4]))
    held = lax.all_gather(outer, "tz", axis=0, tiled=True)
    targets = jnp.stack([own, partner])
    weights = time_weights(targets[:, None] - ring_ids[None, :], total_count)
    partial = jnp.sum(weights.reshape((2, ring) + (1,) * (held.ndim - 1)) * held[None], axis=1)

    faces = jnp.stack([held[:, :, :, -1, :], held[:, :, :, 0, :]], axis=0)
    radial_count = partner_radial.shape[2]
    radial_hot = (partner_radial[..., None] == jnp.arange(radial_count, dtype=jnp.int32)).astype(
        jnp.float32
    )
    remapped = jnp.einsum("szvir,sikr->szvik", faces, radial_hot, precision=lax.Precision.HIGHEST)
    shifts = (targets - own)[:, None, None, None]
    sources = (partner_instance[0][None] + shifts) % total_count
    instance_hot = (sources[..., None] == ring_ids).astype(jnp.float32)
    picked = jnp.sum(instance_hot[:, :, None] * jnp.moveaxis(remapped, 1, -1)[None], axis=-1)

    message = jnp.concatenate([partial[1].reshape(-1), picked[1].reshape(-1)])
    received = lax.ppermute(message, "ty", swap)
    split = partial[0].size
    outer_term = partial[:1] + received[:split].reshape((1,) + partial.shape[1:])
    ghosts = picked[0] + received[split:].reshape(picked.shape[1:])
    early_term = jnp.concatenate(
        [outer_term[:, :, :, :edge], jnp.zeros_like(inner_term), outer_term[:, :, :, edge:]], axis=3
    )
    low_ghost = rotate_velocity(ghosts[0][None], -1.0)
    high_ghost = rotate_velocity(ghosts[1][None], 1.0)

    extended = extended_2(state, (("space", 2),), 1)
    up_i = extended[:, :, 2:]
    down_i = extended[:, :, :-2]
    spatial = section_spatial(state, eddy_visc, jacobians, up_i, down_i, low_ghost, high_ghost)
    step = SECTION_ALPHA * pseudo_step[None, None]
    early, spatial = lax.optimization_barrier((base - step * (spatial + early_term), spatial))
    rows = slice(edge, pitch - edge)
    inner_out = base[:, :, :, rows] - step[:, :, :, rows] * (spatial[:, :, :, rows] + inner_term)
    return early.at[:, :, :, rows].set(inner_out)


def solution(mesh):
    devices = mesh.devices
    cells = devices.shape[1]
    split_mesh = Mesh(
        devices.reshape(devices.shape[0] // Y_PARTS, Y_PARTS, cells), ("tz", "ty", "space")
    )
    time_axes = ("tz", "ty")
    return jax.shard_map(
        per_device,
        mesh=split_mesh,
        in_specs=(
            P(time_axes, None, "space", None, None),
            P(time_axes, None, "space", None, None),
            P("space", None, None),
            P("space", None, None),
            P(),
            P(None, "space", None),
            P(time_axes, None, "space", None),
        ),
        out_specs=P(time_axes, None, "space", None, None),
        check_vma=False,
    )
```

```python
import math

import jax
import jax.numpy as jnp
from jax import lax
from jax.sharding import Mesh
from jax.sharding import PartitionSpec as P

SECTION_ALPHA = 0.5
PITCH_ANGLE = 2.0 * math.pi / 36.0
NYQUIST_DAMP = 2.0
Y_PARTS = 2


def extended_2(block, sides, width):
    for axis, dim in sides:
        count = lax.axis_size(axis)
        forward = [(i, i + 1) for i in range(count - 1)]
        backward = [(target, source) for source, target in forward]
        low = lax.ppermute(
            lax.slice_in_dim(block, block.shape[dim] - width, None, axis=dim), axis, forward
        )
        high = lax.ppermute(lax.slice_in_dim(block, 0, width, axis=dim), axis, backward)
        block = jnp.concatenate([low, block, high], axis=dim)
    return block


def time_weights(offset, count):
    offset = offset % count
    angle = math.pi * offset.astype(jnp.float32) / count
    parity = jnp.where(offset % 2 == 1, 1.0, -1.0).astype(jnp.float32)
    sine = jnp.where(offset == 0, 1.0, jnp.sin(angle))
    spectral = 0.5 * parity * jnp.cos(angle) / sine - NYQUIST_DAMP * parity / count
    return jnp.where(offset == 0, NYQUIST_DAMP / count, spectral)


def rotate_velocity(values, turn):
    cosine = math.cos(PITCH_ANGLE)
    sine = turn * math.sin(PITCH_ANGLE)
    second = values[:, 2]
    third = values[:, 3]
    return jnp.stack(
        [
            values[:, 0],
            values[:, 1],
            cosine * second - sine * third,
            sine * second + cosine * third,
            values[:, 4],
        ],
        axis=1,
    )


def section_spatial(state, eddy_visc, jacobians, up_i, down_i, low_ghost, high_ghost):
    up_j = jnp.concatenate([state[:, :, :, 1:], high_ghost[:, :, :, None]], axis=3)
    down_j = jnp.concatenate([low_ghost[:, :, :, None], state[:, :, :, :-1]], axis=3)
    zeros = jnp.zeros(state.shape[:4] + (1,), state.dtype)
    up_k = jnp.concatenate([state[..., 1:], zeros], axis=4)
    down_k = jnp.concatenate([zeros, state[..., :-1]], axis=4)
    diffs = [(up_i - down_i) * 0.5, (up_j - down_j) * 0.5, (up_k - down_k) * 0.5]
    flux = None
    for direction, diff in enumerate(diffs):
        for source in range(state.shape[1]):
            column = jacobians[direction, :, source].reshape((1, -1) + (1,) * (state.ndim - 2))
            term = column * diff[:, source : source + 1]
            flux = term if flux is None else flux + term
    laplace = up_i + down_i + up_j + down_j + up_k + down_k - 6.0 * state
    return flux - eddy_visc[None, None] * laplace


def per_device(state, base, pseudo_step, eddy_visc, jacobians, partner_radial, partner_instance):
    ring = lax.axis_size("tz")
    total_count = ring * Y_PARTS
    z = lax.axis_index("tz")
    y = lax.axis_index("ty")
    own = Y_PARTS * z + y
    partner = own + 1 - 2 * y
    swap = [(i, Y_PARTS - 1 - i) for i in range(Y_PARTS)]
    ring_ids = Y_PARTS * jnp.arange(ring, dtype=jnp.int32) + y
    pitch = state.shape[3]
    edge = pitch // 4

    inner = state[:, :, :, edge : 2 * edge]
    other = lax.ppermute(inner, "ty", swap)
    expand = (ring,) + (1,) * (inner.ndim - 1)
    own_weights = time_weights(ring_ids - own, total_count).reshape(expand)
    partner_weights = time_weights(ring_ids - partner, total_count).reshape(expand)
    contributions = own_weights * inner + partner_weights * other
    inner_term = lax.psum_scatter(contributions, "tz", scatter_dimension=0, tiled=True)

    outer = jnp.concatenate([state[:, :, :, :edge], state[:, :, :, 2 * edge :]], axis=3)
    held = lax.all_gather(outer, "tz", axis=0, tiled=True)
    targets = jnp.stack([own, partner])
    weights = time_weights(targets[:, None] - ring_ids[None, :], total_count)
    partial = jnp.sum(weights.reshape((2, ring) + (1,) * (held.ndim - 1)) * held[None], axis=1)

    faces = jnp.stack([held[:, :, :, -1, :], held[:, :, :, 0, :]], axis=0)
    radial_count = partner_radial.shape[2]
    radial_hot = (partner_radial[..., None] == jnp.arange(radial_count, dtype=jnp.int32)).astype(
        jnp.float32
    )
    remapped = jnp.einsum("szvir,sikr->szvik", faces, radial_hot, precision=lax.Precision.HIGHEST)
    shifts = (targets - own)[:, None, None, None]
    sources = (partner_instance[0][None] + shifts) % total_count
    instance_hot = (sources[..., None] == ring_ids).astype(jnp.float32)
    picked = jnp.sum(instance_hot[:, :, None] * jnp.moveaxis(remapped, 1, -1)[None], axis=-1)

    message = jnp.concatenate([partial[1].reshape(-1), picked[1].reshape(-1)])
    received = lax.ppermute(message, "ty", swap)
    split = partial[0].size
    outer_term = partial[:1] + received[:split].reshape((1,) + partial.shape[1:])
    ghosts = picked[0] + received[split:].reshape(picked.shape[1:])
    early_term = jnp.concatenate(
        [outer_term[:, :, :, :edge], jnp.zeros_like(inner_term), outer_term[:, :, :, edge:]], axis=3
    )
    low_ghost = rotate_velocity(ghosts[0][None], -1.0)
    high_ghost = rotate_velocity(ghosts[1][None], 1.0)

    extended = extended_2(state, (("space", 2),), 1)
    up_i = extended[:, :, 2:]
    down_i = extended[:, :, :-2]
    spatial = section_spatial(state, eddy_visc, jacobians, up_i, down_i, low_ghost, high_ghost)
    step = SECTION_ALPHA * pseudo_step[None, None]
    early, spatial = lax.optimization_barrier((base - step * (spatial + early_term), spatial))
    rows = slice(edge, 2 * edge)
    inner_out = base[:, :, :, rows] - step[:, :, :, rows] * (spatial[:, :, :, rows] + inner_term)
    return early.at[:, :, :, rows].set(inner_out)


def solution(mesh):
    devices = mesh.devices
    cells = devices.shape[1]
    split_mesh = Mesh(
        devices.reshape(devices.shape[0] // Y_PARTS, Y_PARTS, cells), ("tz", "ty", "space")
    )
    time_axes = ("tz", "ty")
    return jax.shard_map(
        per_device,
        mesh=split_mesh,
        in_specs=(
            P(time_axes, None, "space", None, None),
            P(time_axes, None, "space", None, None),
            P("space", None, None),
            P("space", None, None),
            P(),
            P(None, "space", None),
            P(time_axes, None, "space", None),
        ),
        out_specs=P(time_axes, None, "space", None, None),
        check_vma=False,
    )
```

```python
import math

import jax
import jax.numpy as jnp
from jax import lax
from jax.sharding import Mesh
from jax.sharding import PartitionSpec as P

SECTION_ALPHA = 0.5
PITCH_ANGLE = 2.0 * math.pi / 36.0
NYQUIST_DAMP = 2.0
Y_PARTS = 2


def extended_2(block, sides, width):
    for axis, dim in sides:
        count = lax.axis_size(axis)
        forward = [(i, i + 1) for i in range(count - 1)]
        backward = [(target, source) for source, target in forward]
        low = lax.ppermute(
            lax.slice_in_dim(block, block.shape[dim] - width, None, axis=dim), axis, forward
        )
        high = lax.ppermute(lax.slice_in_dim(block, 0, width, axis=dim), axis, backward)
        block = jnp.concatenate([low, block, high], axis=dim)
    return block


def time_weights(offset, count):
    offset = offset % count
    angle = math.pi * offset.astype(jnp.float32) / count
    parity = jnp.where(offset % 2 == 1, 1.0, -1.0).astype(jnp.float32)
    sine = jnp.where(offset == 0, 1.0, jnp.sin(angle))
    spectral = 0.5 * parity * jnp.cos(angle) / sine - NYQUIST_DAMP * parity / count
    return jnp.where(offset == 0, NYQUIST_DAMP / count, spectral)


def rotate_velocity(values, turn):
    cosine = math.cos(PITCH_ANGLE)
    sine = turn * math.sin(PITCH_ANGLE)
    second = values[:, 2]
    third = values[:, 3]
    return jnp.stack(
        [
            values[:, 0],
            values[:, 1],
            cosine * second - sine * third,
            sine * second + cosine * third,
            values[:, 4],
        ],
        axis=1,
    )


def section_spatial(state, eddy_visc, jacobians, up_i, down_i, low_ghost, high_ghost):
    up_j = jnp.concatenate([state[:, :, :, 1:], high_ghost[:, :, :, None]], axis=3)
    down_j = jnp.concatenate([low_ghost[:, :, :, None], state[:, :, :, :-1]], axis=3)
    zeros = jnp.zeros(state.shape[:4] + (1,), state.dtype)
    up_k = jnp.concatenate([state[..., 1:], zeros], axis=4)
    down_k = jnp.concatenate([zeros, state[..., :-1]], axis=4)
    diffs = [(up_i - down_i) * 0.5, (up_j - down_j) * 0.5, (up_k - down_k) * 0.5]
    flux = None
    for direction, diff in enumerate(diffs):
        for source in range(state.shape[1]):
            column = jacobians[direction, :, source].reshape((1, -1) + (1,) * (state.ndim - 2))
            term = column * diff[:, source : source + 1]
            flux = term if flux is None else flux + term
    laplace = up_i + down_i + up_j + down_j + up_k + down_k - 6.0 * state
    return flux - eddy_visc[None, None] * laplace


def per_device(state, base, pseudo_step, eddy_visc, jacobians, partner_radial, partner_instance):
    ring = lax.axis_size("tz")
    total_count = ring * Y_PARTS
    z = lax.axis_index("tz")
    y = lax.axis_index("ty")
    own = Y_PARTS * z + y
    partner = own + 1 - 2 * y
    swap = [(i, Y_PARTS - 1 - i) for i in range(Y_PARTS)]
    ring_ids = Y_PARTS * jnp.arange(ring, dtype=jnp.int32) + y
    pitch = state.shape[3]
    edge = pitch // 4

    other = lax.ppermute(state, "ty", swap)
    expand = (ring,) + (1,) * (state.ndim - 1)
    own_weights = time_weights(ring_ids - own, total_count).reshape(expand)
    partner_weights = time_weights(ring_ids - partner, total_count).reshape(expand)
    contributions = own_weights * state + partner_weights * other
    time_term = lax.psum_scatter(contributions, "tz", scatter_dimension=0, tiled=True)

    faces_here = jnp.stack([state[:, :, :, -1, :], state[:, :, :, 0, :]], axis=1)
    faces = jnp.moveaxis(lax.all_gather(faces_here, "tz", axis=0, tiled=True), 1, 0)
    targets = jnp.stack([own, partner])

    radial_count = partner_radial.shape[2]
    radial_hot = (partner_radial[..., None] == jnp.arange(radial_count, dtype=jnp.int32)).astype(
        jnp.float32
    )
    remapped = jnp.einsum("szvir,sikr->szvik", faces, radial_hot, precision=lax.Precision.HIGHEST)
    shifts = (targets - own)[:, None, None, None]
    sources = (partner_instance[0][None] + shifts) % total_count
    instance_hot = (sources[..., None] == ring_ids).astype(jnp.float32)
    picked = jnp.sum(instance_hot[:, :, None] * jnp.moveaxis(remapped, 1, -1)[None], axis=-1)
    ghosts = picked[0] + lax.ppermute(picked[1], "ty", swap)
    low_ghost = rotate_velocity(ghosts[0][None], -1.0)
    high_ghost = rotate_velocity(ghosts[1][None], 1.0)

    extended = extended_2(state, (("space", 2),), 1)
    up_i = extended[:, :, 2:]
    down_i = extended[:, :, :-2]
    spatial = lax.optimization_barrier(
        section_spatial(state, eddy_visc, jacobians, up_i, down_i, low_ghost, high_ghost)
    )
    return base - SECTION_ALPHA * pseudo_step[None, None] * (spatial + time_term)


def solution(mesh):
    devices = mesh.devices
    cells = devices.shape[1]
    split_mesh = Mesh(
        devices.reshape(devices.shape[0] // Y_PARTS, Y_PARTS, cells), ("tz", "ty", "space")
    )
    time_axes = ("tz", "ty")
    return jax.shard_map(
        per_device,
        mesh=split_mesh,
        in_specs=(
            P(time_axes, None, "space", None, None),
            P(time_axes, None, "space", None, None),
            P("space", None, None),
            P("space", None, None),
            P(),
            P(None, "space", None),
            P(time_axes, None, "space", None),
        ),
        out_specs=P(time_axes, None, "space", None, None),
        check_vma=False,
    )
```
